128 devices in a mesh: dp: 16 (over z, y_lo, core), space: 8 (over x, y_hi).
Axes of the slice: x: 4, y: 4 (y_hi: 2, y_lo: 2; y = y_hi * 2 + y_lo), z: 4, core: 2. Of those that a mesh axis runs over, the one named last changes fastest.
Arguments:
- decoder_input: bfloat16 [16, 64, 16, 16, 128], P('dp', None, 'space'), may hold values from -6 to 6
- cotangent: bfloat16 [16, 64, 16, 16, 128], P('dp', None, 'space'), may hold values from -6 to 6
- encoder_input: bfloat16 [16, 64, 16, 16, 128], P('dp', None, 'space'), may hold values from -6 to 6
- decoder_weights: bfloat16 [2, 27, 4096], replicated, may hold values from -0.15625 to 0.15625
- other_grads: bfloat16 [16, 8, 12, 27, 4096], P('dp', 'space'), may hold values from -384 to 384
- assignment: int32 [12], replicated, may hold values from 0 to 31, as said below
- moment_first: float32 [32, 27, 4096], P('dp', None, 'space'), may hold values from -4 to 4
- moment_second: float32 [32, 27, 4096], P('dp', None, 'space'), may hold values from 0.02 to 2
- master_weights: float32 [32, 27, 4096], P('dp', None, 'space'), may hold values from -0.15625 to 0.15625
Outputs:
- input_grad: bfloat16 [16, 64, 16, 16, 128], P('dp', None, 'space')
- encoder_out: bfloat16 [16, 64, 16, 16, 128], P('dp', None, 'space')
- new_params: bfloat16 [12, 27, 4096], replicated
- new_first: float32 [32, 27, 4096], P('dp', None, 'space')
- new_second: float32 [32, 27, 4096], P('dp', None, 'space')
- new_master: float32 [32, 27, 4096], P('dp', None, 'space')
The draws below stay inside these ranges and needn't reach their ends.
Inputs may be any that keep to these rules, and one draw needn't show every extreme that they name: `assignment`: the values are distinct; value j places the tensor with owner j // 2 in that owner's slot j % 2; some owner holds 2 tensors.
All inputs are finite; a program needn't handle non-finite values.
Results may differ from the reference program's by a relative error of at most 0.005.
Values may be sent and summed in bfloat16 or wider, within the bound.
No kernel may reach another device: no remote copies, remote signals or barrier semaphores. Data moves between devices by JAX's collectives and lax.ppermute only.
A program may use at most 128 MiB of HBM per device.

```python
import math
import jax
import jax.numpy as jnp
from jax import lax

C = 64
CX = 2
NY = 16
NZ = 128
NT = 12
SLOTS = 2
NX = 16
ALL_SLOTS = 32
N_DP = 16
N_SPACE = 8


def draw_assignment(key, part):
    total_slots = N_DP * SLOTS
    key_owner, key_order, key_shuffle = jax.random.split(key, 3)
    owner = jax.random.randint(key_owner, (), 0, N_DP)
    order = jax.random.permutation(key_order, total_slots)
    ranked = jnp.argsort(order).astype(jnp.int32)
    slot_ids = jnp.arange(total_slots, dtype=jnp.int32)
    in_owner = slot_ids // SLOTS == owner
    scores = jnp.where(in_owner, slot_ids - 4 * total_slots, ranked)
    scores = jnp.where((slot_ids == 0) & jnp.logical_not(in_owner), -3 * total_slots, scores)
    scores = jnp.where((slot_ids == total_slots - 1) & jnp.logical_not(in_owner), -2 * total_slots, scores)
    chosen = jnp.argsort(scores)[:NT].astype(jnp.int32)
    return jax.random.permutation(key_shuffle, chosen).astype(jnp.int32)


def block_levels(stream_key, dims, pieces, smallest, high):
    gain = 1.0
    for position, blocks in pieces:
        steps = jax.random.uniform(jax.random.fold_in(jax.random.fold_in(stream_key, 6), position), (blocks,), jnp.float32, smallest / len(pieces), high / len(pieces))
        gain = gain * jnp.repeat(jnp.exp(steps), dims[position] // blocks).reshape((-1,) + (1,) * (len(dims) - 1 - position))
    return gain


def normal_values(stream_key, extent, deviation, limit, cuts=(), held_as=jnp.bfloat16):
    array = deviation * jax.random.normal(stream_key, extent, jnp.float32)
    if cuts:
        array = array * block_levels(stream_key, extent, cuts, -0.22, 0.18)
    return jnp.clip(array, -limit, limit).astype(held_as)


def setup_inputs(seed: int = 0) -> dict:
    seeds = jax.random.split(jax.random.key(seed), 10)
    decoder_input = normal_values(seeds[0], (N_DP, C, NX, NY, NZ), 1.0, 6.0, ((0, 16), (2, 8)))
    cotangent = normal_values(seeds[1], (N_DP, C, NX, NY, NZ), 1.0, 6.0, ((0, 16), (2, 8)))
    encoder_input = normal_values(seeds[2], (N_DP, C, NX, NY, NZ), 1.0, 6.0, ((0, 16), (2, 8)))
    decoder_weights = normal_values(seeds[3], (2, 27, C * C), (27 * C) ** -0.5, 0.15625)
    other_grads = normal_values(seeds[4], (N_DP, N_SPACE, NT, 27, C * C), ((CX * NY * NZ) ** 0.5), 384.0, ((0, 16), (1, 8)))
    assignment = draw_assignment(jax.random.fold_in(seeds[9], 71), 0)
    moment_first = normal_values(seeds[6], (ALL_SLOTS, 27, C * C), 0.3, 4.0, ((0, 16), (2, 8)), jnp.float32)
    moment_second = jnp.clip(jnp.exp(math.log(2.0) - 4.6051702 * jax.random.uniform(seeds[7], (ALL_SLOTS, 27, C * C), jnp.float32) ** block_levels(seeds[7], (ALL_SLOTS, 27, C * C), ((0, 16), (2, 8)), -0.2, 0.2)), 0.02, 2.0)
    master_weights = normal_values(seeds[8], (ALL_SLOTS, 27, C * C), (27 * C) ** -0.5, 0.15625, ((0, 16), (2, 8)), jnp.float32)
    return {"decoder_input": decoder_input, "cotangent": cotangent, "encoder_input": encoder_input, "decoder_weights": decoder_weights, "other_grads": other_grads, "assignment": assignment, "moment_first": moment_first, "moment_second": moment_second, "master_weights": master_weights}


learn_rate = 0.002
decay_rate = 0.1
epsilon = 1e-08
bias_one = 1.0 - (0.9 ** 50) ** 2
bias_two = 1.0 - (0.999 ** 50) ** 2
tap_offsets = [(a, b, c) for a in (-1, 0, 1) for b in (-1, 0, 1) for c in (-1, 0, 1)]

def moved(field, shift_x, shift_y, shift_z):
    return jnp.roll(field, (-shift_x, -shift_y, -shift_z), axis=(1, 2, 3))

def forward_conv(field, kernel):
    result = jnp.zeros(field.shape, jnp.float32)
    for tap_number, (shift_x, shift_y, shift_z) in enumerate(tap_offsets):
        result = result + jnp.einsum('oi,ixyz->oxyz', kernel[tap_number].astype(jnp.float32), moved(field, shift_x, shift_y, shift_z).astype(jnp.float32))
    return result

def transposed_conv(grads, kernel):
    result = jnp.zeros(grads.shape, jnp.float32)
    for tap_number, (shift_x, shift_y, shift_z) in enumerate(tap_offsets):
        result = result + jnp.einsum('oi,oxyz->ixyz', kernel[tap_number].astype(jnp.float32), moved(grads, -shift_x, -shift_y, -shift_z).astype(jnp.float32))
    return result

def weight_grad(grads, field):
    parts = []
    for shift_x, shift_y, shift_z in tap_offsets:
        parts.append(jnp.einsum('oxyz,ixyz->oi', grads.astype(jnp.float32), moved(field, shift_x, shift_y, shift_z).astype(jnp.float32)))
    return jnp.stack(parts)

def reference(decoder_input, cotangent, encoder_input, decoder_weights, other_grads, assignment, moment_first, moment_second, master_weights):
    kernel_a = decoder_weights[0].reshape(27, C, C)
    kernel_b = decoder_weights[1].reshape(27, C, C)

    def per_box(items):
        dec_field, cot_field = items
        preact = forward_conv(dec_field, kernel_a)
        sigma = jax.nn.sigmoid(preact)
        hidden = (preact * sigma).astype(jnp.bfloat16)
        grad_b = weight_grad(cot_field, hidden)
        grad_hidden = transposed_conv(cot_field, kernel_b)
        grad_pre = (grad_hidden * sigma * (1.0 + preact * (1.0 - sigma))).astype(jnp.bfloat16)
        grad_a = weight_grad(grad_pre, dec_field)
        in_grad = transposed_conv(grad_pre, kernel_a).astype(jnp.bfloat16)
        return (in_grad, grad_a, grad_b)
    input_grad, grads_a, grads_b = lax.map(per_box, (decoder_input, cotangent))
    summed = lax.optimization_barrier(jnp.sum(other_grads, axis=(0, 1), dtype=jnp.float32))
    summed = summed.at[0].add(lax.optimization_barrier(jnp.sum(grads_a, axis=0)).reshape(27, C * C))
    summed = summed.at[1].add(lax.optimization_barrier(jnp.sum(grads_b, axis=0)).reshape(27, C * C))
    totals = summed / (N_DP * NX * NY * NZ) ** 0.5
    slot_grads = jnp.zeros((N_DP * SLOTS, 27, C * C), jnp.float32).at[assignment].set(totals)
    new_first = 0.9 * moment_first + 0.1 * slot_grads
    new_second = 0.999 * moment_second + 0.001 * slot_grads * slot_grads
    update = new_first / bias_one / (jnp.sqrt(new_second / bias_two) + epsilon)
    new_master = master_weights - learn_rate * (update + decay_rate * master_weights)
    new_params = new_master[assignment].astype(jnp.bfloat16)
    kernel_c = new_params[2].reshape(27, C, C)
    kernel_d = new_params[3].reshape(27, C, C)

    def encode(enc_field):
        first = forward_conv(enc_field, kernel_c)
        activ = (first * jax.nn.sigmoid(first)).astype(jnp.bfloat16)
        return (enc_field.astype(jnp.float32) + forward_conv(activ, kernel_d)).astype(jnp.bfloat16)
    encoder_out = lax.map(encode, encoder_input)
    return (input_grad, encoder_out, new_params, new_first, new_second, new_master)
```

```python
import math

import jax
import jax.numpy as jnp
from jax import lax
from jax.sharding import PartitionSpec as P

learn_rate = 0.002
decay_rate = 0.1
epsilon = 1e-08
bias_one = 1.0 - (0.9**50) ** 2
bias_two = 1.0 - (0.999**50) ** 2
volume_dims = ("NCDHW", "OIDHW", "NCDHW")
swapped_dims = ("CNDHW", "OIDHW", "NCDHW")


def padded_2(block, sides, width):
    for axis, dim in sides:
        count = lax.axis_size(axis)
        forward = [(i, i + 1) for i in range(count - 1)]
        forward.append((count - 1, 0))
        backward = [(target, source) for source, target in forward]
        low = lax.ppermute(
            lax.slice_in_dim(block, block.shape[dim] - width, None, axis=dim), axis, forward
        )
        high = lax.ppermute(lax.slice_in_dim(block, 0, width, axis=dim), axis, backward)
        block = jnp.concatenate([low, block, high], axis=dim)
    return block


def widened(field):
    rimmed = padded_2(field, (("space", 1),), 1)
    return jnp.pad(rimmed, ((0, 0), (0, 0), (1, 1), (1, 1)), mode="wrap")


def forward_local(padded, kernel):
    channels = kernel.shape[1]
    weights = kernel.reshape(3, 3, 3, channels, channels).transpose(3, 4, 0, 1, 2)
    result = lax.conv_general_dilated(
        padded[None],
        weights,
        (1, 1, 1),
        "VALID",
        dimension_numbers=volume_dims,
        preferred_element_type=jnp.float32,
    )
    return result[0].reshape(channels, -1)


def backward_local(padded, kernel):
    channels = kernel.shape[1]
    weights = kernel.reshape(3, 3, 3, channels, channels)[::-1, ::-1, ::-1].transpose(4, 3, 0, 1, 2)
    result = lax.conv_general_dilated(
        padded[None],
        weights,
        (1, 1, 1),
        "VALID",
        dimension_numbers=volume_dims,
        preferred_element_type=jnp.float32,
    )
    return result[0].reshape(channels, -1)


def kernel_grad(grad_field, padded):
    channels = grad_field.shape[0]
    result = lax.conv_general_dilated(
        padded[None],
        grad_field[:, None],
        (1, 1, 1),
        "VALID",
        dimension_numbers=swapped_dims,
        preferred_element_type=jnp.float32,
    )
    return result.transpose(2, 3, 4, 1, 0).reshape(27, channels, channels)


def space_scatter(block):
    count = lax.axis_size("space")
    lead = block.shape[:-1]
    split = block.reshape(lead + (count, block.shape[-1] // count))
    split = jnp.moveaxis(split, -2, 0)
    return lax.psum_scatter(split, "space", scatter_dimension=0, tiled=True)[0]


def space_gather(block):
    count = lax.axis_size("space")
    lead = block.shape[:-1]
    whole = lax.all_gather(block, "space", axis=0, tiled=False)
    whole = jnp.moveaxis(whole, 0, -2)
    return whole.reshape(lead + (count * block.shape[-1],))


def adamw(grads, first, second, master):
    new_first = 0.9 * first + 0.1 * grads
    new_second = 0.999 * second + 0.001 * grads * grads
    update = new_first / bias_one / (jnp.sqrt(new_second / bias_two) + epsilon)
    new_master = master - learn_rate * (update + decay_rate * master)
    return new_first, new_second, new_master


def owner_rows(grads, assign, owner, first, second, master):
    slot_count = first.shape[0]
    local = assign % slot_count
    pick = lambda state: jnp.take(state, local, axis=0)
    rows = adamw(grads, pick(first), pick(second), pick(master))[2].astype(jnp.bfloat16)
    mine = (assign // slot_count == owner)[:, None, None]
    return jnp.where(mine, rows, jnp.zeros_like(rows))


def per_device(
    decoder_input,
    cotangent,
    encoder_input,
    decoder_weights,
    other_grads,
    assignment,
    moment_first,
    moment_second,
    master_weights,
):
    field_shape = decoder_input.shape[1:]
    channels = field_shape[0]
    thick = field_shape[1]
    kernel_a = decoder_weights[0].reshape(27, channels, channels)
    kernel_b = decoder_weights[1].reshape(27, channels, channels)
    dec_field = decoder_input[0]
    dec_wide = widened(dec_field)
    preact = forward_local(dec_wide, kernel_a)
    sigma = jax.nn.sigmoid(preact)
    hidden = (preact * sigma).astype(jnp.bfloat16).reshape(field_shape)
    cot_field = cotangent[0]
    grad_b = kernel_grad(cot_field, widened(hidden))
    grad_hidden = backward_local(widened(cot_field), kernel_b)
    grad_pre = (
        (grad_hidden * sigma * (1.0 + preact * (1.0 - sigma)))
        .astype(jnp.bfloat16)
        .reshape(field_shape)
    )
    grad_a = kernel_grad(grad_pre, dec_wide)
    input_grad = backward_local(widened(grad_pre), kernel_a)
    input_grad = input_grad.astype(jnp.bfloat16).reshape((1,) + field_shape)
    replicas = lax.axis_size("dp")
    slabs = lax.axis_size("space")
    scale = 1.0 / math.sqrt(replicas * thick * slabs * field_shape[2] * field_shape[3])
    owner = lax.axis_index("dp")
    other_tot = lax.psum(space_scatter(other_grads[0, 0]), "dp").astype(jnp.float32)
    enc_rows = owner_rows(
        other_tot[2:4] * scale, assignment[2:4], owner, moment_first, moment_second, master_weights
    )
    enc_params = space_gather(lax.psum(enc_rows, "dp"))
    kernel_c = enc_params[0].reshape(27, channels, channels)
    kernel_d = enc_params[1].reshape(27, channels, channels)
    ab_grads = jnp.stack([grad_a.reshape(27, -1), grad_b.reshape(27, -1)]).astype(jnp.bfloat16)
    ab_tot = lax.psum(space_scatter(ab_grads), "dp").astype(jnp.float32)
    totals = jnp.concatenate([other_tot[:2] + ab_tot, other_tot[2:]]) * scale
    slot_count = moment_first.shape[0]
    slot_ids = owner * slot_count + jnp.arange(slot_count)
    match = assignment[None, :] == slot_ids[:, None]
    owned = jnp.sum(jnp.where(match[:, :, None, None], totals[None], 0.0), axis=1)
    new_first, new_second, new_master = adamw(owned, moment_first, moment_second, master_weights)
    late = jnp.array([0, 1] + list(range(4, assignment.shape[0])))
    late_assign = assignment[late]
    late_local = jnp.take(new_master.astype(jnp.bfloat16), late_assign % slot_count, axis=0)
    late_rows = jnp.where(
        (late_assign // slot_count == owner)[:, None, None], late_local, jnp.zeros_like(late_local)
    )
    late_params = space_gather(lax.psum(late_rows, "dp"))
    new_params = jnp.concatenate([late_params[:2], enc_params, late_params[2:]])
    enc_field = encoder_input[0]
    first = forward_local(widened(enc_field), kernel_c)
    activ = (first * jax.nn.sigmoid(first)).astype(jnp.bfloat16).reshape(field_shape)
    second = forward_local(widened(activ), kernel_d)
    encoder_out = (enc_field.reshape(channels, -1).astype(jnp.float32) + second).astype(
        jnp.bfloat16
    )
    encoder_out = encoder_out.reshape((1,) + field_shape)
    return (input_grad, encoder_out, new_params, new_first, new_second, new_master)


def solution(mesh):
    in_specs = (
        P("dp", None, "space", None, None),
        P("dp", None, "space", None, None),
        P("dp", None, "space", None, None),
        P(),
        P("dp", "space", None, None, None),
        P(),
        P("dp", None, "space"),
        P("dp", None, "space"),
        P("dp", None, "space"),
    )
    out_specs = (
        P("dp", None, "space", None, None),
        P("dp", None, "space", None, None),
        P(),
        P("dp", None, "space"),
        P("dp", None, "space"),
        P("dp", None, "space"),
    )
    return jax.shard_map(
        per_device, mesh=mesh, in_specs=in_specs, out_specs=out_specs, check_vma=False
    )
```

```python
import math

import jax
import jax.numpy as jnp
from jax import lax
from jax.sharding import PartitionSpec as P

learn_rate = 0.002
decay_rate = 0.1
epsilon = 1e-08
bias_one = 1.0 - (0.9**50) ** 2
bias_two = 1.0 - (0.999**50) ** 2
volume_dims = ("NCDHW", "OIDHW", "NCDHW")
swapped_dims = ("CNDHW", "OIDHW", "NCDHW")


def padded_2(block, sides, width):
    for axis, dim in sides:
        count = lax.axis_size(axis)
        forward = [(i, i + 1) for i in range(count - 1)]
        forward.append((count - 1, 0))
        backward = [(target, source) for source, target in forward]
        low = lax.ppermute(
            lax.slice_in_dim(block, block.shape[dim] - width, None, axis=dim), axis, forward
        )
        high = lax.ppermute(lax.slice_in_dim(block, 0, width, axis=dim), axis, backward)
        block = jnp.concatenate([low, block, high], axis=dim)
    return block


def widened(field):
    rimmed = padded_2(field, (("space", 1),), 1)
    return jnp.pad(rimmed, ((0, 0), (0, 0), (1, 1), (1, 1)), mode="wrap")


def forward_local(padded, kernel):
    channels = kernel.shape[1]
    weights = kernel.reshape(3, 3, 3, channels, channels).transpose(3, 4, 0, 1, 2)
    result = lax.conv_general_dilated(
        padded[None],
        weights,
        (1, 1, 1),
        "VALID",
        dimension_numbers=volume_dims,
        preferred_element_type=jnp.float32,
    )
    return result[0].reshape(channels, -1)


def backward_local(padded, kernel):
    channels = kernel.shape[1]
    weights = kernel.reshape(3, 3, 3, channels, channels)[::-1, ::-1, ::-1].transpose(4, 3, 0, 1, 2)
    result = lax.conv_general_dilated(
        padded[None],
        weights,
        (1, 1, 1),
        "VALID",
        dimension_numbers=volume_dims,
        preferred_element_type=jnp.float32,
    )
    return result[0].reshape(channels, -1)


def kernel_grad(grad_field, padded):
    channels = grad_field.shape[0]
    result = lax.conv_general_dilated(
        padded[None],
        grad_field[:, None],
        (1, 1, 1),
        "VALID",
        dimension_numbers=swapped_dims,
        preferred_element_type=jnp.float32,
    )
    return result.transpose(2, 3, 4, 1, 0).reshape(27, channels, channels)


def space_reduce(block):
    count = lax.axis_size("space")
    lead = block.shape[:-1]
    split = block.reshape(lead + (count, block.shape[-1] // count))
    split = jnp.moveaxis(split, -2, 0)
    arrived = lax.all_to_all(split, "space", 0, 0, tiled=True)
    return jnp.sum(arrived.astype(jnp.float32), axis=0)


def space_gather(block):
    count = lax.axis_size("space")
    lead = block.shape[:-1]
    copies = jnp.broadcast_to(block[None], (count,) + block.shape)
    whole = lax.all_to_all(copies, "space", 0, 0, tiled=True)
    whole = jnp.moveaxis(whole, 0, -2)
    return whole.reshape(lead + (count * block.shape[-1],))


def per_device(
    decoder_input,
    cotangent,
    encoder_input,
    decoder_weights,
    other_grads,
    assignment,
    moment_first,
    moment_second,
    master_weights,
):
    field_shape = decoder_input.shape[1:]
    channels = field_shape[0]
    thick = field_shape[1]
    kernel_a = decoder_weights[0].reshape(27, channels, channels)
    kernel_b = decoder_weights[1].reshape(27, channels, channels)
    dec_field = decoder_input[0]
    dec_wide = widened(dec_field)
    preact = forward_local(dec_wide, kernel_a)
    sigma = jax.nn.sigmoid(preact)
    hidden = (preact * sigma).astype(jnp.bfloat16).reshape(field_shape)
    cot_field = cotangent[0]
    grad_b = kernel_grad(cot_field, widened(hidden))
    grad_hidden = backward_local(widened(cot_field), kernel_b)
    grad_pre = (
        (grad_hidden * sigma * (1.0 + preact * (1.0 - sigma)))
        .astype(jnp.bfloat16)
        .reshape(field_shape)
    )
    grad_a = kernel_grad(grad_pre, dec_wide)
    input_grad = backward_local(widened(grad_pre), kernel_a)
    input_grad = input_grad.astype(jnp.bfloat16).reshape((1,) + field_shape)
    replicas = lax.axis_size("dp")
    slabs = lax.axis_size("space")
    scale = 1.0 / math.sqrt(replicas * thick * slabs * field_shape[2] * field_shape[3])
    local_grads = other_grads[0, 0].astype(jnp.float32)
    local_grads = local_grads.at[0].add(grad_a.reshape(27, -1))
    local_grads = local_grads.at[1].add(grad_b.reshape(27, -1))
    column_sums = space_reduce(local_grads.astype(jnp.bfloat16))
    slot_count = moment_first.shape[0]
    every_slot = replicas * slot_count
    padded_grads = (
        jnp.zeros((every_slot,) + column_sums.shape[1:], jnp.bfloat16)
        .at[assignment]
        .set(column_sums.astype(jnp.bfloat16))
    )
    arrived = lax.all_to_all(padded_grads, "dp", 0, 0, tiled=True)
    arrived = arrived.reshape((replicas, slot_count) + arrived.shape[1:])
    owned = jnp.sum(arrived.astype(jnp.float32), axis=0) * scale
    new_first = 0.9 * moment_first + 0.1 * owned
    new_second = 0.999 * moment_second + 0.001 * owned * owned
    update = new_first / bias_one / (jnp.sqrt(new_second / bias_two) + epsilon)
    new_master = master_weights - learn_rate * (update + decay_rate * master_weights)
    mine_rounded = new_master.astype(jnp.bfloat16)
    gathered = lax.all_gather(mine_rounded, "dp", axis=0, tiled=True)
    picked = jnp.take(gathered, assignment, axis=0)
    new_params = space_gather(picked)
    kernel_c = new_params[2].reshape(27, channels, channels)
    kernel_d = new_params[3].reshape(27, channels, channels)
    enc_field = encoder_input[0]
    first = forward_local(widened(enc_field), kernel_c)
    activ = (first * jax.nn.sigmoid(first)).astype(jnp.bfloat16).reshape(field_shape)
    second = forward_local(widened(activ), kernel_d)
    encoder_out = (enc_field.reshape(channels, -1).astype(jnp.float32) + second).astype(
        jnp.bfloat16
    )
    encoder_out = encoder_out.reshape((1,) + field_shape)
    return (input_grad, encoder_out, new_params, new_first, new_second, new_master)


def solution(mesh):
    in_specs = (
        P("dp", None, "space", None, None),
        P("dp", None, "space", None, None),
        P("dp", None, "space", None, None),
        P(),
        P("dp", "space", None, None, None),
        P(),
        P("dp", None, "space"),
        P("dp", None, "space"),
        P("dp", None, "space"),
    )
    out_specs = (
        P("dp", None, "space", None, None),
        P("dp", None, "space", None, None),
        P(),
        P("dp", None, "space"),
        P("dp", None, "space"),
        P("dp", None, "space"),
    )
    return jax.shard_map(
        per_device, mesh=mesh, in_specs=in_specs, out_specs=out_specs, check_vma=False
    )
```

```python
import math

import jax
import jax.numpy as jnp
from jax import lax
from jax.sharding import PartitionSpec as P

learn_rate = 0.002
decay_rate = 0.1
epsilon = 1e-08
bias_one = 1.0 - (0.9**50) ** 2
bias_two = 1.0 - (0.999**50) ** 2
volume_dims = ("NCDHW", "OIDHW", "NCDHW")
swapped_dims = ("CNDHW", "OIDHW", "NCDHW")


def padded_2(block, sides, width):
    for axis, dim in sides:
        count = lax.axis_size(axis)
        forward = [(i, i + 1) for i in range(count - 1)]
        forward.append((count - 1, 0))
        backward = [(target, source) for source, target in forward]
        low = lax.ppermute(
            lax.slice_in_dim(block, block.shape[dim] - width, None, axis=dim), axis, forward
        )
        high = lax.ppermute(lax.slice_in_dim(block, 0, width, axis=dim), axis, backward)
        block = jnp.concatenate([low, block, high], axis=dim)
    return block


def widened(field):
    rimmed = padded_2(field, (("space", 1),), 1)
    return jnp.pad(rimmed, ((0, 0), (0, 0), (1, 1), (1, 1)), mode="wrap")


def forward_local(padded, kernel):
    channels = kernel.shape[1]
    weights = kernel.reshape(3, 3, 3, channels, channels).transpose(3, 4, 0, 1, 2)
    result = lax.conv_general_dilated(
        padded[None],
        weights,
        (1, 1, 1),
        "VALID",
        dimension_numbers=volume_dims,
        preferred_element_type=jnp.float32,
    )
    return result[0].reshape(channels, -1)


def backward_local(padded, kernel):
    channels = kernel.shape[1]
    weights = kernel.reshape(3, 3, 3, channels, channels)[::-1, ::-1, ::-1].transpose(4, 3, 0, 1, 2)
    result = lax.conv_general_dilated(
        padded[None],
        weights,
        (1, 1, 1),
        "VALID",
        dimension_numbers=volume_dims,
        preferred_element_type=jnp.float32,
    )
    return result[0].reshape(channels, -1)


def kernel_grad(grad_field, padded):
    channels = grad_field.shape[0]
    result = lax.conv_general_dilated(
        padded[None],
        grad_field[:, None],
        (1, 1, 1),
        "VALID",
        dimension_numbers=swapped_dims,
        preferred_element_type=jnp.float32,
    )
    return result.transpose(2, 3, 4, 1, 0).reshape(27, channels, channels)


def space_reduce(block):
    count = lax.axis_size("space")
    lead = block.shape[:-1]
    split = block.reshape(lead + (count, block.shape[-1] // count))
    split = jnp.moveaxis(split, -2, 0)
    arrived = lax.all_to_all(split, "space", 0, 0, tiled=True)
    return jnp.sum(arrived.astype(jnp.float32), axis=0)


def space_gather(block):
    count = lax.axis_size("space")
    lead = block.shape[:-1]
    copies = jnp.broadcast_to(block[None], (count,) + block.shape)
    whole = lax.all_to_all(copies, "space", 0, 0, tiled=True)
    whole = jnp.moveaxis(whole, 0, -2)
    return whole.reshape(lead + (count * block.shape[-1],))


def dp_reduce(rows, assign, slot_count):
    replicas = lax.axis_size("dp")
    padded = (
        jnp.zeros((replicas * slot_count,) + rows.shape[1:], jnp.bfloat16)
        .at[assign]
        .set(rows.astype(jnp.bfloat16))
    )
    arrived = lax.all_to_all(padded, "dp", 0, 0, tiled=True)
    arrived = arrived.reshape((replicas, slot_count) + arrived.shape[1:])
    return jnp.sum(arrived.astype(jnp.float32), axis=0)


def dp_gather(block):
    replicas = lax.axis_size("dp")
    copies = jnp.broadcast_to(block[None], (replicas,) + block.shape)
    whole = lax.all_to_all(copies, "dp", 0, 0, tiled=True)
    return whole.reshape((replicas * block.shape[0],) + block.shape[1:])


def dp_pick(rows, owners):
    replicas = lax.axis_size("dp")
    copies = jnp.broadcast_to(rows[None], (replicas,) + rows.shape)
    whole = lax.all_to_all(copies, "dp", 0, 0, tiled=True)
    return whole[owners, jnp.arange(rows.shape[0])]


def adamw(grads, first, second, master):
    new_first = 0.9 * first + 0.1 * grads
    new_second = 0.999 * second + 0.001 * grads * grads
    update = new_first / bias_one / (jnp.sqrt(new_second / bias_two) + epsilon)
    new_master = master - learn_rate * (update + decay_rate * master)
    return new_first, new_second, new_master


def per_device(
    decoder_input,
    cotangent,
    encoder_input,
    decoder_weights,
    other_grads,
    assignment,
    moment_first,
    moment_second,
    master_weights,
):
    field_shape = decoder_input.shape[1:]
    channels = field_shape[0]
    thick = field_shape[1]
    kernel_a = decoder_weights[0].reshape(27, channels, channels)
    kernel_b = decoder_weights[1].reshape(27, channels, channels)
    dec_field = decoder_input[0]
    dec_wide = widened(dec_field)
    preact = forward_local(dec_wide, kernel_a)
    sigma = jax.nn.sigmoid(preact)
    hidden = (preact * sigma).astype(jnp.bfloat16).reshape(field_shape)
    cot_field = cotangent[0]
    grad_b = kernel_grad(cot_field, widened(hidden))
    grad_hidden = backward_local(widened(cot_field), kernel_b)
    grad_pre = (
        (grad_hidden * sigma * (1.0 + preact * (1.0 - sigma)))
        .astype(jnp.bfloat16)
        .reshape(field_shape)
    )
    grad_a = kernel_grad(grad_pre, dec_wide)
    input_grad = backward_local(widened(grad_pre), kernel_a)
    input_grad = input_grad.astype(jnp.bfloat16).reshape((1,) + field_shape)
    replicas = lax.axis_size("dp")
    slabs = lax.axis_size("space")
    scale = 1.0 / math.sqrt(replicas * thick * slabs * field_shape[2] * field_shape[3])
    owner = lax.axis_index("dp")
    slot_count = moment_first.shape[0]
    other_sums = space_reduce(other_grads[0, 0])
    early_owned = dp_reduce(other_sums, assignment, slot_count)
    enc_assign = assignment[2:4]
    enc_local = enc_assign % slot_count
    pick = lambda state: jnp.take(state, enc_local, axis=0)
    enc_grads = jnp.take(early_owned, enc_local, axis=0) * scale
    enc_rows = adamw(enc_grads, pick(moment_first), pick(moment_second), pick(master_weights))[2]
    enc_rows = dp_pick(enc_rows.astype(jnp.bfloat16), enc_assign // slot_count)
    enc_params = space_gather(enc_rows)
    ab_grads = jnp.stack([grad_a.reshape(27, -1), grad_b.reshape(27, -1)]).astype(jnp.bfloat16)
    ab_sums = space_reduce(ab_grads)
    late_owned = dp_reduce(ab_sums, assignment[:2], slot_count)
    owned = (early_owned + late_owned) * scale
    new_first, new_second, new_master = adamw(owned, moment_first, moment_second, master_weights)
    gathered = dp_gather(new_master.astype(jnp.bfloat16))
    late = jnp.array([0, 1] + list(range(4, assignment.shape[0])))
    late_params = space_gather(jnp.take(gathered, assignment[late], axis=0))
    new_params = jnp.concatenate([late_params[:2], enc_params, late_params[2:]])
    kernel_c = enc_params[0].reshape(27, channels, channels)
    kernel_d = enc_params[1].reshape(27, channels, channels)
    enc_field = encoder_input[0]
    first = forward_local(widened(enc_field), kernel_c)
    activ = (first * jax.nn.sigmoid(first)).astype(jnp.bfloat16).reshape(field_shape)
    second = forward_local(widened(activ), kernel_d)
    encoder_out = (enc_field.reshape(channels, -1).astype(jnp.float32) + second).astype(
        jnp.bfloat16
    )
    encoder_out = encoder_out.reshape((1,) + field_shape)
    return (input_grad, encoder_out, new_params, new_first, new_second, new_master)


def solution(mesh):
    in_specs = (
        P("dp", None, "space", None, None),
        P("dp", None, "space", None, None),
        P("dp", None, "space", None, None),
        P(),
        P("dp", "space", None, None, None),
        P(),
        P("dp", None, "space"),
        P("dp", None, "space"),
        P("dp", None, "space"),
    )
    out_specs = (
        P("dp", None, "space", None, None),
        P("dp", None, "space", None, None),
        P(),
        P("dp", None, "space"),
        P("dp", None, "space"),
        P("dp", None, "space"),
    )
    return jax.shard_map(
        per_device, mesh=mesh, in_specs=in_specs, out_specs=out_specs, check_vma=False
    )
```

```python
import math

import jax
import jax.numpy as jnp
from jax import lax
from jax.sharding import PartitionSpec as P

learn_rate = 0.002
decay_rate = 0.1
epsilon = 1e-08
bias_one = 1.0 - (0.9**50) ** 2
bias_two = 1.0 - (0.999**50) ** 2
volume_dims = ("NCDHW", "OIDHW", "NCDHW")
swapped_dims = ("CNDHW", "OIDHW", "NCDHW")


def padded_2(block, sides, width):
    for axis, dim in sides:
        count = lax.axis_size(axis)
        forward = [(i, i + 1) for i in range(count - 1)]
        forward.append((count - 1, 0))
        backward = [(target, source) for source, target in forward]
        low = lax.ppermute(
            lax.slice_in_dim(block, block.shape[dim] - width, None, axis=dim), axis, forward
        )
        high = lax.ppermute(lax.slice_in_dim(block, 0, width, axis=dim), axis, backward)
        block = jnp.concatenate([low, block, high], axis=dim)
    return block


def widened(field):
    rimmed = padded_2(field, (("space", 1),), 1)
    return jnp.pad(rimmed, ((0, 0), (0, 0), (1, 1), (1, 1)), mode="wrap")


def forward_local(padded, kernel):
    channels = kernel.shape[1]
    weights = kernel.reshape(3, 3, 3, channels, channels).transpose(3, 4, 0, 1, 2)
    result = lax.conv_general_dilated(
        padded[None],
        weights,
        (1, 1, 1),
        "VALID",
        dimension_numbers=volume_dims,
        preferred_element_type=jnp.float32,
    )
    return result[0].reshape(channels, -1)


def backward_local(padded, kernel):
    channels = kernel.shape[1]
    weights = kernel.reshape(3, 3, 3, channels, channels)[::-1, ::-1, ::-1].transpose(4, 3, 0, 1, 2)
    result = lax.conv_general_dilated(
        padded[None],
        weights,
        (1, 1, 1),
        "VALID",
        dimension_numbers=volume_dims,
        preferred_element_type=jnp.float32,
    )
    return result[0].reshape(channels, -1)


def kernel_grad(grad_field, padded):
    channels = grad_field.shape[0]
    result = lax.conv_general_dilated(
        padded[None],
        grad_field[:, None],
        (1, 1, 1),
        "VALID",
        dimension_numbers=swapped_dims,
        preferred_element_type=jnp.float32,
    )
    return result.transpose(2, 3, 4, 1, 0).reshape(27, channels, channels)


def space_reduce(block):
    count = lax.axis_size("space")
    lead = block.shape[:-1]
    split = block.reshape(lead + (count, block.shape[-1] // count))
    split = jnp.moveaxis(split, -2, 0)
    arrived = lax.all_to_all(split, "space", 0, 0, tiled=True)
    return jnp.sum(arrived.astype(jnp.float32), axis=0)


def space_gather(block):
    count = lax.axis_size("space")
    lead = block.shape[:-1]
    copies = jnp.broadcast_to(block[None], (count,) + block.shape)
    whole = lax.all_to_all(copies, "space", 0, 0, tiled=True)
    whole = jnp.moveaxis(whole, 0, -2)
    return whole.reshape(lead + (count * block.shape[-1],))


def dp_reduce(rows, assign, slot_count):
    replicas = lax.axis_size("dp")
    padded = (
        jnp.zeros((replicas * slot_count,) + rows.shape[1:], jnp.bfloat16)
        .at[assign]
        .set(rows.astype(jnp.bfloat16))
    )
    arrived = lax.all_to_all(padded, "dp", 0, 0, tiled=True)
    arrived = arrived.reshape((replicas, slot_count) + arrived.shape[1:])
    return jnp.sum(arrived.astype(jnp.float32), axis=0)


def dp_gather(block):
    replicas = lax.axis_size("dp")
    copies = jnp.broadcast_to(block[None], (replicas,) + block.shape)
    whole = lax.all_to_all(copies, "dp", 0, 0, tiled=True)
    return whole.reshape((replicas * block.shape[0],) + block.shape[1:])


def dp_pick(rows, owners):
    replicas = lax.axis_size("dp")
    copies = jnp.broadcast_to(rows[None], (replicas,) + rows.shape)
    whole = lax.all_to_all(copies, "dp", 0, 0, tiled=True)
    return whole[owners, jnp.arange(rows.shape[0])]


def adamw(grads, first, second, master):
    new_first = 0.9 * first + 0.1 * grads
    new_second = 0.999 * second + 0.001 * grads * grads
    update = new_first / bias_one / (jnp.sqrt(new_second / bias_two) + epsilon)
    new_master = master - learn_rate * (update + decay_rate * master)
    return new_first, new_second, new_master


def per_device(
    decoder_input,
    cotangent,
    encoder_input,
    decoder_weights,
    other_grads,
    assignment,
    moment_first,
    moment_second,
    master_weights,
):
    field_shape = decoder_input.shape[1:]
    channels = field_shape[0]
    thick = field_shape[1]
    kernel_a = decoder_weights[0].reshape(27, channels, channels)
    kernel_b = decoder_weights[1].reshape(27, channels, channels)
    replicas = lax.axis_size("dp")
    slabs = lax.axis_size("space")
    scale = 1.0 / math.sqrt(replicas * thick * slabs * field_shape[2] * field_shape[3])
    slot_count = moment_first.shape[0]
    other_sums = space_reduce(other_grads[0, 0])
    dec_field = decoder_input[0]
    dec_wide = widened(dec_field)
    preact = forward_local(dec_wide, kernel_a)
    sigma = jax.nn.sigmoid(preact)
    hidden = (preact * sigma).astype(jnp.bfloat16).reshape(field_shape)
    hidden, other_sums = lax.optimization_barrier((hidden, other_sums))
    early_owned = dp_reduce(other_sums, assignment, slot_count)
    cot_field = cotangent[0]
    grad_b = kernel_grad(cot_field, widened(hidden))
    grad_hidden = backward_local(widened(cot_field), kernel_b)
    grad_pre = (
        (grad_hidden * sigma * (1.0 + preact * (1.0 - sigma)))
        .astype(jnp.bfloat16)
        .reshape(field_shape)
    )
    grad_pre, early_owned = lax.optimization_barrier((grad_pre, early_owned))
    early_master = adamw(early_owned * scale, moment_first, moment_second, master_weights)[2]
    early_gathered = dp_gather(early_master.astype(jnp.bfloat16))
    grad_a = kernel_grad(grad_pre, dec_wide)
    pre_wide = widened(grad_pre)
    pre_wide, early_gathered = lax.optimization_barrier((pre_wide, early_gathered))
    enc_params = space_gather(jnp.take(early_gathered, assignment[2:4], axis=0))
    input_grad = backward_local(pre_wide, kernel_a)
    input_grad = input_grad.astype(jnp.bfloat16).reshape((1,) + field_shape)
    rest_params = space_gather(jnp.take(early_gathered, assignment[4:], axis=0))
    ab_grads = jnp.stack([grad_a.reshape(27, -1), grad_b.reshape(27, -1)]).astype(jnp.bfloat16)
    ab_sums = space_reduce(ab_grads)
    late_owned = dp_reduce(ab_sums, assignment[:2], slot_count)
    owned = (early_owned + late_owned) * scale
    new_first, new_second, new_master = adamw(owned, moment_first, moment_second, master_weights)
    ab_assign = assignment[:2]
    ab_rows = jnp.take(new_master.astype(jnp.bfloat16), ab_assign % slot_count, axis=0)
    ab_params = space_gather(dp_pick(ab_rows, ab_assign // slot_count))
    new_params = jnp.concatenate([ab_params, enc_params, rest_params])
    kernel_c = enc_params[0].reshape(27, channels, channels)
    kernel_d = enc_params[1].reshape(27, channels, channels)
    enc_field = encoder_input[0]
    first = forward_local(widened(enc_field), kernel_c)
    activ = (first * jax.nn.sigmoid(first)).astype(jnp.bfloat16).reshape(field_shape)
    second = forward_local(widened(activ), kernel_d)
    encoder_out = (enc_field.reshape(channels, -1).astype(jnp.float32) + second).astype(
        jnp.bfloat16
    )
    encoder_out = encoder_out.reshape((1,) + field_shape)
    return (input_grad, encoder_out, new_params, new_first, new_second, new_master)


def solution(mesh):
    in_specs = (
        P("dp", None, "space", None, None),
        P("dp", None, "space", None, None),
        P("dp", None, "space", None, None),
        P(),
        P("dp", "space", None, None, None),
        P(),
        P("dp", None, "space"),
        P("dp", None, "space"),
        P("dp", None, "space"),
    )
    out_specs = (
        P("dp", None, "space", None, None),
        P("dp", None, "space", None, None),
        P(),
        P("dp", None, "space"),
        P("dp", None, "space"),
        P("dp", None, "space"),
    )
    return jax.shard_map(
        per_device, mesh=mesh, in_specs=in_specs, out_specs=out_specs, check_vma=False
    )
```

```python
import math

import jax
import jax.numpy as jnp
from jax import lax
from jax.sharding import PartitionSpec as P

learn_rate = 0.002
decay_rate = 0.1
epsilon = 1e-08
bias_one = 1.0 - (0.9**50) ** 2
bias_two = 1.0 - (0.999**50) ** 2
volume_dims = ("NCDHW", "OIDHW", "NCDHW")
swapped_dims = ("CNDHW", "OIDHW", "NCDHW")


def padded_2(block, sides, width):
    for axis, dim in sides:
        count = lax.axis_size(axis)
        forward = [(i, i + 1) for i in range(count - 1)]
        forward.append((count - 1, 0))
        backward = [(target, source) for source, target in forward]
        low = lax.ppermute(
            lax.slice_in_dim(block, block.shape[dim] - width, None, axis=dim), axis, forward
        )
        high = lax.ppermute(lax.slice_in_dim(block, 0, width, axis=dim), axis, backward)
        block = jnp.concatenate([low, block, high], axis=dim)
    return block


def widened(field):
    rimmed = padded_2(field, (("space", 1),), 1)
    return jnp.pad(rimmed, ((0, 0), (0, 0), (1, 1), (1, 1)), mode="wrap")


def forward_local(padded, kernel):
    channels = kernel.shape[1]
    weights = kernel.reshape(3, 3, 3, channels, channels).transpose(3, 4, 0, 1, 2)
    result = lax.conv_general_dilated(
        padded[None],
        weights,
        (1, 1, 1),
        "VALID",
        dimension_numbers=volume_dims,
        preferred_element_type=jnp.float32,
    )
    return result[0].reshape(channels, -1)


def backward_local(padded, kernel):
    channels = kernel.shape[1]
    weights = kernel.reshape(3, 3, 3, channels, channels)[::-1, ::-1, ::-1].transpose(4, 3, 0, 1, 2)
    result = lax.conv_general_dilated(
        padded[None],
        weights,
        (1, 1, 1),
        "VALID",
        dimension_numbers=volume_dims,
        preferred_element_type=jnp.float32,
    )
    return result[0].reshape(channels, -1)


def kernel_grad(grad_field, padded):
    channels = grad_field.shape[0]
    result = lax.conv_general_dilated(
        padded[None],
        grad_field[:, None],
        (1, 1, 1),
        "VALID",
        dimension_numbers=swapped_dims,
        preferred_element_type=jnp.float32,
    )
    return result.transpose(2, 3, 4, 1, 0).reshape(27, channels, channels)


def space_reduce(block):
    count = lax.axis_size("space")
    lead = block.shape[:-1]
    split = block.reshape(lead + (count, block.shape[-1] // count))
    split = jnp.moveaxis(split, -2, 0)
    arrived = lax.all_to_all(split, "space", 0, 0, tiled=True)
    return jnp.sum(arrived.astype(jnp.float32), axis=0)


def space_scatter(block):
    count = lax.axis_size("space")
    lead = block.shape[:-1]
    split = block.reshape(lead + (count, block.shape[-1] // count))
    split = jnp.moveaxis(split, -2, 0)
    summed = lax.psum_scatter(split, "space", scatter_dimension=0, tiled=True)[0]
    return summed.astype(jnp.float32)


def space_collect(block):
    count = lax.axis_size("space")
    lead = block.shape[:-1]
    whole = lax.all_gather(block, "space", axis=0, tiled=False)
    whole = jnp.moveaxis(whole, 0, -2)
    return whole.reshape(lead + (count * block.shape[-1],))


def space_gather(block):
    count = lax.axis_size("space")
    lead = block.shape[:-1]
    copies = jnp.broadcast_to(block[None], (count,) + block.shape)
    whole = lax.all_to_all(copies, "space", 0, 0, tiled=True)
    whole = jnp.moveaxis(whole, 0, -2)
    return whole.reshape(lead + (count * block.shape[-1],))


def dp_reduce(rows, assign, slot_count):
    replicas = lax.axis_size("dp")
    padded = (
        jnp.zeros((replicas * slot_count,) + rows.shape[1:], jnp.bfloat16)
        .at[assign]
        .set(rows.astype(jnp.bfloat16))
    )
    arrived = lax.all_to_all(padded, "dp", 0, 0, tiled=True)
    arrived = arrived.reshape((replicas, slot_count) + arrived.shape[1:])
    return jnp.sum(arrived.astype(jnp.float32), axis=0)


def dp_gather(block):
    replicas = lax.axis_size("dp")
    copies = jnp.broadcast_to(block[None], (replicas,) + block.shape)
    whole = lax.all_to_all(copies, "dp", 0, 0, tiled=True)
    return whole.reshape((replicas * block.shape[0],) + block.shape[1:])


def dp_pick(rows, owners):
    replicas = lax.axis_size("dp")
    copies = jnp.broadcast_to(rows[None], (replicas,) + rows.shape)
    whole = lax.all_to_all(copies, "dp", 0, 0, tiled=True)
    return whole[owners, jnp.arange(rows.shape[0])]


def adamw(grads, first, second, master):
    new_first = 0.9 * first + 0.1 * grads
    new_second = 0.999 * second + 0.001 * grads * grads
    update = new_first / bias_one / (jnp.sqrt(new_second / bias_two) + epsilon)
    new_master = master - learn_rate * (update + decay_rate * master)
    return new_first, new_second, new_master


def per_device(
    decoder_input,
    cotangent,
    encoder_input,
    decoder_weights,
    other_grads,
    assignment,
    moment_first,
    moment_second,
    master_weights,
):
    field_shape = decoder_input.shape[1:]
    channels = field_shape[0]
    thick = field_shape[1]
    kernel_a = decoder_weights[0].reshape(27, channels, channels)
    kernel_b = decoder_weights[1].reshape(27, channels, channels)
    replicas = lax.axis_size("dp")
    slabs = lax.axis_size("space")
    scale = 1.0 / math.sqrt(replicas * thick * slabs * field_shape[2] * field_shape[3])
    slot_count = moment_first.shape[0]
    other_sums = space_scatter(other_grads[0, 0])
    dec_field = decoder_input[0]
    dec_wide = widened(dec_field)
    preact = forward_local(dec_wide, kernel_a)
    sigma = jax.nn.sigmoid(preact)
    hidden = (preact * sigma).astype(jnp.bfloat16).reshape(field_shape)
    cot_field = cotangent[0]
    grad_b = kernel_grad(cot_field, widened(hidden))
    grad_hidden = backward_local(widened(cot_field), kernel_b)
    grad_pre = (
        (grad_hidden * sigma * (1.0 + preact * (1.0 - sigma)))
        .astype(jnp.bfloat16)
        .reshape(field_shape)
    )
    grad_pre, other_sums = lax.optimization_barrier((grad_pre, other_sums))
    early_owned = dp_reduce(other_sums, assignment, slot_count)
    early_master = adamw(early_owned * scale, moment_first, moment_second, master_weights)[2]
    early_gathered = dp_gather(early_master.astype(jnp.bfloat16))
    grad_a = kernel_grad(grad_pre, dec_wide)
    enc_params = space_gather(jnp.take(early_gathered, assignment[2:4], axis=0))
    input_grad = backward_local(widened(grad_pre), kernel_a)
    input_grad = input_grad.astype(jnp.bfloat16).reshape((1,) + field_shape)
    rest_params = space_collect(jnp.take(early_gathered, assignment[4:], axis=0))
    ab_grads = jnp.stack([grad_a.reshape(27, -1), grad_b.reshape(27, -1)]).astype(jnp.bfloat16)
    ab_grads, enc_params = lax.optimization_barrier((ab_grads, enc_params))
    ab_sums = space_reduce(ab_grads)
    late_owned = dp_reduce(ab_sums, assignment[:2], slot_count)
    owned = (early_owned + late_owned) * scale
    new_first, new_second, new_master = adamw(owned, moment_first, moment_second, master_weights)
    ab_assign = assignment[:2]
    ab_rows = jnp.take(new_master.astype(jnp.bfloat16), ab_assign % slot_count, axis=0)
    ab_params = space_gather(dp_pick(ab_rows, ab_assign // slot_count))
    new_params = jnp.concatenate([ab_params, enc_params, rest_params])
    kernel_c = enc_params[0].reshape(27, channels, channels)
    kernel_d = enc_params[1].reshape(27, channels, channels)
    enc_field = encoder_input[0]
    first = forward_local(widened(enc_field), kernel_c)
    activ = (first * jax.nn.sigmoid(first)).astype(jnp.bfloat16).reshape(field_shape)
    second = forward_local(widened(activ), kernel_d)
    encoder_out = (enc_field.reshape(channels, -1).astype(jnp.float32) + second).astype(
        jnp.bfloat16
    )
    encoder_out = encoder_out.reshape((1,) + field_shape)
    return (input_grad, encoder_out, new_params, new_first, new_second, new_master)


def solution(mesh):
    in_specs = (
        P("dp", None, "space", None, None),
        P("dp", None, "space", None, None),
        P("dp", None, "space", None, None),
        P(),
        P("dp", "space", None, None, None),
        P(),
        P("dp", None, "space"),
        P("dp", None, "space"),
        P("dp", None, "space"),
    )
    out_specs = (
        P("dp", None, "space", None, None),
        P("dp", None, "space", None, None),
        P(),
        P("dp", None, "space"),
        P("dp", None, "space"),
        P("dp", None, "space"),
    )
    return jax.shard_map(
        per_device, mesh=mesh, in_specs=in_specs, out_specs=out_specs, check_vma=False
    )
```

```python
import math

import jax
import jax.numpy as jnp
from jax import lax
from jax.sharding import PartitionSpec as P

learn_rate = 0.002
decay_rate = 0.1
epsilon = 1e-08
bias_one = 1.0 - (0.9**50) ** 2
bias_two = 1.0 - (0.999**50) ** 2
volume_dims = ("NCDHW", "OIDHW", "NCDHW")
swapped_dims = ("CNDHW", "OIDHW", "NCDHW")


def padded_2(block, sides, width):
    for axis, dim in sides:
        count = lax.axis_size(axis)
        forward = [(i, i + 1) for i in range(count - 1)]
        forward.append((count - 1, 0))
        backward = [(target, source) for source, target in forward]
        low = lax.ppermute(
            lax.slice_in_dim(block, block.shape[dim] - width, None, axis=dim), axis, forward
        )
        high = lax.ppermute(lax.slice_in_dim(block, 0, width, axis=dim), axis, backward)
        block = jnp.concatenate([low, block, high], axis=dim)
    return block


def widened(field):
    rimmed = padded_2(field, (("space", 1),), 1)
    return jnp.pad(rimmed, ((0, 0), (0, 0), (1, 1), (1, 1)), mode="wrap")


def forward_local(padded, kernel):
    channels = kernel.shape[1]
    weights = kernel.reshape(3, 3, 3, channels, channels).transpose(3, 4, 0, 1, 2)
    result = lax.conv_general_dilated(
        padded[None],
        weights,
        (1, 1, 1),
        "VALID",
        dimension_numbers=volume_dims,
        preferred_element_type=jnp.float32,
    )
    return result[0].reshape(channels, -1)


def backward_local(padded, kernel):
    channels = kernel.shape[1]
    weights = kernel.reshape(3, 3, 3, channels, channels)[::-1, ::-1, ::-1].transpose(4, 3, 0, 1, 2)
    result = lax.conv_general_dilated(
        padded[None],
        weights,
        (1, 1, 1),
        "VALID",
        dimension_numbers=volume_dims,
        preferred_element_type=jnp.float32,
    )
    return result[0].reshape(channels, -1)


def kernel_grad(grad_field, padded):
    channels = grad_field.shape[0]
    result = lax.conv_general_dilated(
        padded[None],
        grad_field[:, None],
        (1, 1, 1),
        "VALID",
        dimension_numbers=swapped_dims,
        preferred_element_type=jnp.float32,
    )
    return result.transpose(2, 3, 4, 1, 0).reshape(27, channels, channels)


def space_reduce(block):
    count = lax.axis_size("space")
    lead = block.shape[:-1]
    split = block.reshape(lead + (count, block.shape[-1] // count))
    split = jnp.moveaxis(split, -2, 0)
    arrived = lax.all_to_all(split, "space", 0, 0, tiled=True)
    return jnp.sum(arrived.astype(jnp.float32), axis=0)


def space_collect(block):
    count = lax.axis_size("space")
    lead = block.shape[:-1]
    whole = lax.all_gather(block, "space", axis=0, tiled=False)
    whole = jnp.moveaxis(whole, 0, -2)
    return whole.reshape(lead + (count * block.shape[-1],))


def space_gather(block):
    count = lax.axis_size("space")
    lead = block.shape[:-1]
    copies = jnp.broadcast_to(block[None], (count,) + block.shape)
    whole = lax.all_to_all(copies, "space", 0, 0, tiled=True)
    whole = jnp.moveaxis(whole, 0, -2)
    return whole.reshape(lead + (count * block.shape[-1],))


def dp_reduce(rows, assign, slot_count):
    replicas = lax.axis_size("dp")
    padded = (
        jnp.zeros((replicas * slot_count,) + rows.shape[1:], jnp.bfloat16)
        .at[assign]
        .set(rows.astype(jnp.bfloat16))
    )
    arrived = lax.all_to_all(padded, "dp", 0, 0, tiled=True)
    arrived = arrived.reshape((replicas, slot_count) + arrived.shape[1:])
    return jnp.sum(arrived.astype(jnp.float32), axis=0)


def dp_gather(block):
    replicas = lax.axis_size("dp")
    copies = jnp.broadcast_to(block[None], (replicas,) + block.shape)
    whole = lax.all_to_all(copies, "dp", 0, 0, tiled=True)
    return whole.reshape((replicas * block.shape[0],) + block.shape[1:])


def dp_pick(rows, owners):
    replicas = lax.axis_size("dp")
    copies = jnp.broadcast_to(rows[None], (replicas,) + rows.shape)
    whole = lax.all_to_all(copies, "dp", 0, 0, tiled=True)
    return whole[owners, jnp.arange(rows.shape[0])]


def adamw(grads, first, second, master):
    new_first = 0.9 * first + 0.1 * grads
    new_second = 0.999 * second + 0.001 * grads * grads
    update = new_first / bias_one / (jnp.sqrt(new_second / bias_two) + epsilon)
    new_master = master - learn_rate * (update + decay_rate * master)
    return new_first, new_second, new_master


def per_device(
    decoder_input,
    cotangent,
    encoder_input,
    decoder_weights,
    other_grads,
    assignment,
    moment_first,
    moment_second,
    master_weights,
):
    field_shape = decoder_input.shape[1:]
    channels = field_shape[0]
    thick = field_shape[1]
    kernel_a = decoder_weights[0].reshape(27, channels, channels)
    kernel_b = decoder_weights[1].reshape(27, channels, channels)
    replicas = lax.axis_size("dp")
    slabs = lax.axis_size("space")
    scale = 1.0 / math.sqrt(replicas * thick * slabs * field_shape[2] * field_shape[3])
    slot_count = moment_first.shape[0]
    other_sums = space_reduce(other_grads[0, 0])
    dec_field = decoder_input[0]
    dec_wide = widened(dec_field)
    preact = forward_local(dec_wide, kernel_a)
    sigma = jax.nn.sigmoid(preact)
    hidden = (preact * sigma).astype(jnp.bfloat16).reshape(field_shape)
    hidden, other_sums = lax.optimization_barrier((hidden, other_sums))
    early_owned = dp_reduce(other_sums, assignment, slot_count)
    cot_field = cotangent[0]
    grad_b = kernel_grad(cot_field, widened(hidden))
    grad_hidden = backward_local(widened(cot_field), kernel_b)
    grad_pre = (
        (grad_hidden * sigma * (1.0 + preact * (1.0 - sigma)))
        .astype(jnp.bfloat16)
        .reshape(field_shape)
    )
    grad_pre, early_owned = lax.optimization_barrier((grad_pre, early_owned))
    early_master = adamw(early_owned * scale, moment_first, moment_second, master_weights)[2]
    early_gathered = dp_gather(early_master.astype(jnp.bfloat16))
    grad_a = kernel_grad(grad_pre, dec_wide)
    enc_params = space_gather(jnp.take(early_gathered, assignment[2:4], axis=0))
    input_grad = backward_local(widened(grad_pre), kernel_a)
    input_grad = input_grad.astype(jnp.bfloat16).reshape((1,) + field_shape)
    rest_params = space_collect(jnp.take(early_gathered, assignment[4:], axis=0))
    ab_grads = jnp.stack([grad_a.reshape(27, -1), grad_b.reshape(27, -1)]).astype(jnp.bfloat16)
    ab_grads, enc_params = lax.optimization_barrier((ab_grads, enc_params))
    ab_sums = space_reduce(ab_grads)
    late_owned = dp_reduce(ab_sums, assignment[:2], slot_count)
    owned = (early_owned + late_owned) * scale
    new_first, new_second, new_master = adamw(owned, moment_first, moment_second, master_weights)
    ab_assign = assignment[:2]
    ab_rows = jnp.take(new_master.astype(jnp.bfloat16), ab_assign % slot_count, axis=0)
    ab_params = space_gather(dp_pick(ab_rows, ab_assign // slot_count))
    new_params = jnp.concatenate([ab_params, enc_params, rest_params])
    kernel_c = enc_params[0].reshape(27, channels, channels)
    kernel_d = enc_params[1].reshape(27, channels, channels)
    enc_field = encoder_input[0]
    first = forward_local(widened(enc_field), kernel_c)
    activ = (first * jax.nn.sigmoid(first)).astype(jnp.bfloat16).reshape(field_shape)
    second = forward_local(widened(activ), kernel_d)
    encoder_out = (enc_field.reshape(channels, -1).astype(jnp.float32) + second).astype(
        jnp.bfloat16
    )
    encoder_out = encoder_out.reshape((1,) + field_shape)
    return (input_grad, encoder_out, new_params, new_first, new_second, new_master)


def solution(mesh):
    in_specs = (
        P("dp", None, "space", None, None),
        P("dp", None, "space", None, None),
        P("dp", None, "space", None, None),
        P(),
        P("dp", "space", None, None, None),
        P(),
        P("dp", None, "space"),
        P("dp", None, "space"),
        P("dp", None, "space"),
    )
    out_specs = (
        P("dp", None, "space", None, None),
        P("dp", None, "space", None, None),
        P(),
        P("dp", None, "space"),
        P("dp", None, "space"),
        P("dp", None, "space"),
    )
    return jax.shard_map(
        per_device, mesh=mesh, in_specs=in_specs, out_specs=out_specs, check_vma=False
    )
```

```python
import math

import jax
import jax.numpy as jnp
from jax import lax
from jax.sharding import PartitionSpec as P

learn_rate = 0.002
decay_rate = 0.1
epsilon = 1e-08
bias_one = 1.0 - (0.9**50) ** 2
bias_two = 1.0 - (0.999**50) ** 2
volume_dims = ("NCDHW", "OIDHW", "NCDHW")
swapped_dims = ("CNDHW", "OIDHW", "NCDHW")


def padded_2(block, sides, width):
    for axis, dim in sides:
        count = lax.axis_size(axis)
        forward = [(i, i + 1) for i in range(count - 1)]
        forward.append((count - 1, 0))
        backward = [(target, source) for source, target in forward]
        low = lax.ppermute(
            lax.slice_in_dim(block, block.shape[dim] - width, None, axis=dim), axis, forward
        )
        high = lax.ppermute(lax.slice_in_dim(block, 0, width, axis=dim), axis, backward)
        block = jnp.concatenate([low, block, high], axis=dim)
    return block


def widened(field):
    rimmed = padded_2(field, (("space", 1),), 1)
    return jnp.pad(rimmed, ((0, 0), (0, 0), (1, 1), (1, 1)), mode="wrap")


def forward_local(padded, kernel):
    channels = kernel.shape[1]
    weights = kernel.reshape(3, 3, 3, channels, channels).transpose(3, 4, 0, 1, 2)
    result = lax.conv_general_dilated(
        padded[None],
        weights,
        (1, 1, 1),
        "VALID",
        dimension_numbers=volume_dims,
        preferred_element_type=jnp.float32,
    )
    return result[0].reshape(channels, -1)


def backward_local(padded, kernel):
    channels = kernel.shape[1]
    weights = kernel.reshape(3, 3, 3, channels, channels)[::-1, ::-1, ::-1].transpose(4, 3, 0, 1, 2)
    result = lax.conv_general_dilated(
        padded[None],
        weights,
        (1, 1, 1),
        "VALID",
        dimension_numbers=volume_dims,
        preferred_element_type=jnp.float32,
    )
    return result[0].reshape(channels, -1)


def kernel_grad(grad_field, padded):
    channels = grad_field.shape[0]
    result = lax.conv_general_dilated(
        padded[None],
        grad_field[:, None],
        (1, 1, 1),
        "VALID",
        dimension_numbers=swapped_dims,
        preferred_element_type=jnp.float32,
    )
    return result.transpose(2, 3, 4, 1, 0).reshape(27, channels, channels)


def space_reduce(block):
    count = lax.axis_size("space")
    lead = block.shape[:-1]
    split = block.reshape(lead + (count, block.shape[-1] // count))
    split = jnp.moveaxis(split, -2, 0)
    arrived = lax.all_to_all(split, "space", 0, 0, tiled=True)
    return jnp.sum(arrived.astype(jnp.float32), axis=0)


def space_collect(block):
    count = lax.axis_size("space")
    lead = block.shape[:-1]
    whole = lax.all_gather(block, "space", axis=0, tiled=False)
    whole = jnp.moveaxis(whole, 0, -2)
    return whole.reshape(lead + (count * block.shape[-1],))


def space_gather(block):
    count = lax.axis_size("space")
    lead = block.shape[:-1]
    copies = jnp.broadcast_to(block[None], (count,) + block.shape)
    whole = lax.all_to_all(copies, "space", 0, 0, tiled=True)
    whole = jnp.moveaxis(whole, 0, -2)
    return whole.reshape(lead + (count * block.shape[-1],))


def dp_reduce(rows, assign, slot_count):
    replicas = lax.axis_size("dp")
    padded = (
        jnp.zeros((replicas * slot_count,) + rows.shape[1:], jnp.bfloat16)
        .at[assign]
        .set(rows.astype(jnp.bfloat16))
    )
    arrived = lax.all_to_all(padded, "dp", 0, 0, tiled=True)
    arrived = arrived.reshape((replicas, slot_count) + arrived.shape[1:])
    return jnp.sum(arrived.astype(jnp.float32), axis=0)


def dp_gather(block):
    replicas = lax.axis_size("dp")
    copies = jnp.broadcast_to(block[None], (replicas,) + block.shape)
    whole = lax.all_to_all(copies, "dp", 0, 0, tiled=True)
    return whole.reshape((replicas * block.shape[0],) + block.shape[1:])


def dp_pick(rows, owners):
    replicas = lax.axis_size("dp")
    copies = jnp.broadcast_to(rows[None], (replicas,) + rows.shape)
    whole = lax.all_to_all(copies, "dp", 0, 0, tiled=True)
    return whole[owners, jnp.arange(rows.shape[0])]


def adamw(grads, first, second, master):
    new_first = 0.9 * first + 0.1 * grads
    new_second = 0.999 * second + 0.001 * grads * grads
    update = new_first / bias_one / (jnp.sqrt(new_second / bias_two) + epsilon)
    new_master = master - learn_rate * (update + decay_rate * master)
    return new_first, new_second, new_master


def per_device(
    decoder_input,
    cotangent,
    encoder_input,
    decoder_weights,
    other_grads,
    assignment,
    moment_first,
    moment_second,
    master_weights,
):
    field_shape = decoder_input.shape[1:]
    channels = field_shape[0]
    thick = field_shape[1]
    kernel_a = decoder_weights[0].reshape(27, channels, channels)
    kernel_b = decoder_weights[1].reshape(27, channels, channels)
    replicas = lax.axis_size("dp")
    slabs = lax.axis_size("space")
    scale = 1.0 / math.sqrt(replicas * thick * slabs * field_shape[2] * field_shape[3])
    slot_count = moment_first.shape[0]
    other_sums = space_reduce(other_grads[0, 0])
    dec_field = decoder_input[0]
    dec_wide = widened(dec_field)
    preact = forward_local(dec_wide, kernel_a)
    sigma = jax.nn.sigmoid(preact)
    hidden = (preact * sigma).astype(jnp.bfloat16).reshape(field_shape)
    hidden, other_sums = lax.optimization_barrier((hidden, other_sums))
    early_owned = dp_reduce(other_sums, assignment, slot_count)
    cot_field = cotangent[0]
    grad_b = kernel_grad(cot_field, widened(hidden))
    grad_hidden = backward_local(widened(cot_field), kernel_b)
    grad_pre = (
        (grad_hidden * sigma * (1.0 + preact * (1.0 - sigma)))
        .astype(jnp.bfloat16)
        .reshape(field_shape)
    )
    grad_pre, early_owned = lax.optimization_barrier((grad_pre, early_owned))
    early_master = adamw(early_owned * scale, moment_first, moment_second, master_weights)[2]
    early_gathered = dp_gather(early_master.astype(jnp.bfloat16))
    grad_a = kernel_grad(grad_pre, dec_wide)
    pre_wide = widened(grad_pre)
    pre_wide, early_gathered = lax.optimization_barrier((pre_wide, early_gathered))
    enc_params = space_gather(jnp.take(early_gathered, assignment[2:4], axis=0))
    input_grad = backward_local(pre_wide, kernel_a)
    input_grad = input_grad.astype(jnp.bfloat16).reshape((1,) + field_shape)
    rest_params = space_collect(jnp.take(early_gathered, assignment[4:], axis=0))
    ab_grads = jnp.stack([grad_a.reshape(27, -1), grad_b.reshape(27, -1)]).astype(jnp.bfloat16)
    ab_grads, enc_params = lax.optimization_barrier((ab_grads, enc_params))
    ab_sums = space_reduce(ab_grads)
    late_owned = dp_reduce(ab_sums, assignment[:2], slot_count)
    owned = (early_owned + late_owned) * scale
    new_first, new_second, new_master = adamw(owned, moment_first, moment_second, master_weights)
    ab_assign = assignment[:2]
    ab_rows = jnp.take(new_master.astype(jnp.bfloat16), ab_assign % slot_count, axis=0)
    ab_params = space_gather(dp_pick(ab_rows, ab_assign // slot_count))
    new_params = jnp.concatenate([ab_params, enc_params, rest_params])
    kernel_c = enc_params[0].reshape(27, channels, channels)
    kernel_d = enc_params[1].reshape(27, channels, channels)
    enc_field = encoder_input[0]
    first = forward_local(widened(enc_field), kernel_c)
    activ = (first * jax.nn.sigmoid(first)).astype(jnp.bfloat16).reshape(field_shape)
    second = forward_local(widened(activ), kernel_d)
    encoder_out = (enc_field.reshape(channels, -1).astype(jnp.float32) + second).astype(
        jnp.bfloat16
    )
    encoder_out = encoder_out.reshape((1,) + field_shape)
    return (input_grad, encoder_out, new_params, new_first, new_second, new_master)


def solution(mesh):
    in_specs = (
        P("dp", None, "space", None, None),
        P("dp", None, "space", None, None),
        P("dp", None, "space", None, None),
        P(),
        P("dp", "space", None, None, None),
        P(),
        P("dp", None, "space"),
        P("dp", None, "space"),
        P("dp", None, "space"),
    )
    out_specs = (
        P("dp", None, "space", None, None),
        P("dp", None, "space", None, None),
        P(),
        P("dp", None, "space"),
        P("dp", None, "space"),
        P("dp", None, "space"),
    )
    return jax.shard_map(
        per_device, mesh=mesh, in_specs=in_specs, out_specs=out_specs, check_vma=False
    )
```

```python
import math

import jax
import jax.numpy as jnp
from jax import lax
from jax.sharding import PartitionSpec as P

learn_rate = 0.002
decay_rate = 0.1
epsilon = 1e-08
bias_one = 1.0 - (0.9**50) ** 2
bias_two = 1.0 - (0.999**50) ** 2
volume_dims = ("NCDHW", "OIDHW", "NCDHW")
swapped_dims = ("CNDHW", "OIDHW", "NCDHW")


def padded_2(block, sides, width):
    for axis, dim in sides:
        count = lax.axis_size(axis)
        forward = [(i, i + 1) for i in range(count - 1)]
        forward.append((count - 1, 0))
        backward = [(target, source) for source, target in forward]
        low = lax.ppermute(
            lax.slice_in_dim(block, block.shape[dim] - width, None, axis=dim), axis, forward
        )
        high = lax.ppermute(lax.slice_in_dim(block, 0, width, axis=dim), axis, backward)
        block = jnp.concatenate([low, block, high], axis=dim)
    return block


def widened(field):
    rimmed = padded_2(field, (("space", 1),), 1)
    return jnp.pad(rimmed, ((0, 0), (0, 0), (1, 1), (1, 1)), mode="wrap")


def forward_local(padded, kernel):
    channels = kernel.shape[1]
    weights = kernel.reshape(3, 3, 3, channels, channels).transpose(3, 4, 0, 1, 2)
    result = lax.conv_general_dilated(
        padded[None],
        weights,
        (1, 1, 1),
        "VALID",
        dimension_numbers=volume_dims,
        preferred_element_type=jnp.float32,
    )
    return result[0].reshape(channels, -1)


def backward_local(padded, kernel):
    channels = kernel.shape[1]
    weights = kernel.reshape(3, 3, 3, channels, channels)[::-1, ::-1, ::-1].transpose(4, 3, 0, 1, 2)
    result = lax.conv_general_dilated(
        padded[None],
        weights,
        (1, 1, 1),
        "VALID",
        dimension_numbers=volume_dims,
        preferred_element_type=jnp.float32,
    )
    return result[0].reshape(channels, -1)


def kernel_grad(grad_field, padded):
    channels = grad_field.shape[0]
    result = lax.conv_general_dilated(
        padded[None],
        grad_field[:, None],
        (1, 1, 1),
        "VALID",
        dimension_numbers=swapped_dims,
        preferred_element_type=jnp.float32,
    )
    return result.transpose(2, 3, 4, 1, 0).reshape(27, channels, channels)


def space_reduce(block):
    count = lax.axis_size("space")
    lead = block.shape[:-1]
    split = block.reshape(lead + (count, block.shape[-1] // count))
    split = jnp.moveaxis(split, -2, 0)
    arrived = lax.all_to_all(split, "space", 0, 0, tiled=True)
    return jnp.sum(arrived.astype(jnp.float32), axis=0)


def space_gather(block):
    count = lax.axis_size("space")
    lead = block.shape[:-1]
    copies = jnp.broadcast_to(block[None], (count,) + block.shape)
    whole = lax.all_to_all(copies, "space", 0, 0, tiled=True)
    whole = jnp.moveaxis(whole, 0, -2)
    return whole.reshape(lead + (count * block.shape[-1],))


def dp_reduce(rows, assign, slot_count):
    replicas = lax.axis_size("dp")
    padded = (
        jnp.zeros((replicas * slot_count,) + rows.shape[1:], jnp.bfloat16)
        .at[assign]
        .set(rows.astype(jnp.bfloat16))
    )
    arrived = lax.all_to_all(padded, "dp", 0, 0, tiled=True)
    arrived = arrived.reshape((replicas, slot_count) + arrived.shape[1:])
    return jnp.sum(arrived.astype(jnp.float32), axis=0)


def dp_gather(block):
    replicas = lax.axis_size("dp")
    copies = jnp.broadcast_to(block[None], (replicas,) + block.shape)
    whole = lax.all_to_all(copies, "dp", 0, 0, tiled=True)
    return whole.reshape((replicas * block.shape[0],) + block.shape[1:])


def dp_pick(rows, owners):
    replicas = lax.axis_size("dp")
    copies = jnp.broadcast_to(rows[None], (replicas,) + rows.shape)
    whole = lax.all_to_all(copies, "dp", 0, 0, tiled=True)
    return whole[owners, jnp.arange(rows.shape[0])]


def adamw(grads, first, second, master):
    new_first = 0.9 * first + 0.1 * grads
    new_second = 0.999 * second + 0.001 * grads * grads
    update = new_first / bias_one / (jnp.sqrt(new_second / bias_two) + epsilon)
    new_master = master - learn_rate * (update + decay_rate * master)
    return new_first, new_second, new_master


def per_device(
    decoder_input,
    cotangent,
    encoder_input,
    decoder_weights,
    other_grads,
    assignment,
    moment_first,
    moment_second,
    master_weights,
):
    field_shape = decoder_input.shape[1:]
    channels = field_shape[0]
    thick = field_shape[1]
    kernel_a = decoder_weights[0].reshape(27, channels, channels)
    kernel_b = decoder_weights[1].reshape(27, channels, channels)
    slot_count = moment_first.shape[0]
    other_sums = space_reduce(other_grads[0, 0])
    dec_field = decoder_input[0]
    dec_wide = widened(dec_field)
    preact = forward_local(dec_wide, kernel_a)
    sigma = jax.nn.sigmoid(preact)
    hidden = (preact * sigma).astype(jnp.bfloat16).reshape(field_shape)
    hidden, other_sums = lax.optimization_barrier((hidden, other_sums))
    early_owned = dp_reduce(other_sums, assignment, slot_count)
    cot_field = cotangent[0]
    grad_b = kernel_grad(cot_field, widened(hidden))
    grad_hidden = backward_local(widened(cot_field), kernel_b)
    grad_pre = (
        (grad_hidden * sigma * (1.0 + preact * (1.0 - sigma)))
        .astype(jnp.bfloat16)
        .reshape(field_shape)
    )
    grad_pre, early_owned = lax.optimization_barrier((grad_pre, early_owned))
    grad_a = kernel_grad(grad_pre, dec_wide)
    input_grad = backward_local(widened(grad_pre), kernel_a)
    input_grad = input_grad.astype(jnp.bfloat16).reshape((1,) + field_shape)
    replicas = lax.axis_size("dp")
    slabs = lax.axis_size("space")
    scale = 1.0 / math.sqrt(replicas * thick * slabs * field_shape[2] * field_shape[3])
    owner = lax.axis_index("dp")
    enc_assign = assignment[2:4]
    enc_local = enc_assign % slot_count
    pick = lambda state: jnp.take(state, enc_local, axis=0)
    enc_grads = jnp.take(early_owned, enc_local, axis=0) * scale
    enc_rows = adamw(enc_grads, pick(moment_first), pick(moment_second), pick(master_weights))[2]
    enc_rows = dp_pick(enc_rows.astype(jnp.bfloat16), enc_assign // slot_count)
    enc_params = space_gather(enc_rows)
    ab_grads = jnp.stack([grad_a.reshape(27, -1), grad_b.reshape(27, -1)]).astype(jnp.bfloat16)
    ab_sums = space_reduce(ab_grads)
    late_owned = dp_reduce(ab_sums, assignment[:2], slot_count)
    owned = (early_owned + late_owned) * scale
    new_first, new_second, new_master = adamw(owned, moment_first, moment_second, master_weights)
    gathered = dp_gather(new_master.astype(jnp.bfloat16))
    late = jnp.array([0, 1] + list(range(4, assignment.shape[0])))
    late_params = space_gather(jnp.take(gathered, assignment[late], axis=0))
    new_params = jnp.concatenate([late_params[:2], enc_params, late_params[2:]])
    kernel_c = enc_params[0].reshape(27, channels, channels)
    kernel_d = enc_params[1].reshape(27, channels, channels)
    enc_field = encoder_input[0]
    first = forward_local(widened(enc_field), kernel_c)
    activ = (first * jax.nn.sigmoid(first)).astype(jnp.bfloat16).reshape(field_shape)
    second = forward_local(widened(activ), kernel_d)
    encoder_out = (enc_field.reshape(channels, -1).astype(jnp.float32) + second).astype(
        jnp.bfloat16
    )
    encoder_out = encoder_out.reshape((1,) + field_shape)
    return (input_grad, encoder_out, new_params, new_first, new_second, new_master)


def solution(mesh):
    in_specs = (
        P("dp", None, "space", None, None),
        P("dp", None, "space", None, None),
        P("dp", None, "space", None, None),
        P(),
        P("dp", "space", None, None, None),
        P(),
        P("dp", None, "space"),
        P("dp", None, "space"),
        P("dp", None, "space"),
    )
    out_specs = (
        P("dp", None, "space", None, None),
        P("dp", None, "space", None, None),
        P(),
        P("dp", None, "space"),
        P("dp", None, "space"),
        P("dp", None, "space"),
    )
    return jax.shard_map(
        per_device, mesh=mesh, in_specs=in_specs, out_specs=out_specs, check_vma=False
    )
```
